768 devices in a mesh: blk: 96 (over y, z), grp: 8 (over x, core).
Axes of the slice: x: 4, y: 8, z: 12, core: 2. Of those that a mesh axis runs over, the one named last changes fastest.
Arguments:
- points: float32 [49152, 256], P(('blk', 'grp')), may hold values from -6 to 6
- centroids: float32 [135168, 256], P(('blk', 'grp')), may hold values from -6 to 6
- counts: float32 [135168], P(('blk', 'grp')), may hold values from 1 to 20
- assign: int32 [49152], P(('blk', 'grp')), may hold values from 0 to 1407, as said below
Outputs:
- nearest: float32 [49152], P(('blk', 'grp'))
- new_centroids: float32 [135168, 256], P(('blk', 'grp'))
- new_counts: float32 [135168], P(('blk', 'grp'))
The draws below stay inside these ranges and needn't reach their ends.
Inputs may be any that keep to these rules, and one draw needn't show every extreme that they name: Every point of coarse cell b names a centroid of that cell. Of the 64 points of one device, at most 32 name centroids held by one device of its group along grp (owner assign // 176); every device sends exactly 32 to one owner, and in every group one owner receives 32 from each of the group's devices.
All inputs are finite; a program needn't handle non-finite values.
Results may differ from the reference program's by a relative error of at most 0.0028.
Values may be sent and summed in bfloat16 or wider, within the bound.
No kernel may reach another device: no remote copies, remote signals or barrier semaphores. Data moves between devices by JAX's collectives and lax.ppermute only.
A program may use at most 32 MiB of HBM per device.

```python
import math
import jax
import jax.numpy as jnp
from jax import lax

D = 256
CEN_DEV = 176
PTS_DEV = 64
CAP = 32
K_CELL = 1408
CENTROIDS = 135168
POINTS = 49152
N_BLK = 96
N_GRP = 8


def draw_assign(key, part):
    devices_all = N_BLK * N_GRP
    busy_owner = jax.random.randint(jax.random.fold_in(key, 11), (N_BLK,), 0, N_GRP)
    busy_device = jnp.repeat(busy_owner, N_GRP)
    offsets = jax.random.randint(jax.random.fold_in(key, 12), (devices_all, PTS_DEV - CAP), 1, N_GRP)
    others = (busy_device[:, None] + offsets) % N_GRP
    busy_rows = jnp.broadcast_to(busy_device[:, None], (devices_all, CAP))
    owner_index = jnp.concatenate([busy_rows, others], axis=1)
    local_index = jax.random.randint(jax.random.fold_in(key, 13), (devices_all, PTS_DEV), 0, CEN_DEV)
    cell_index = owner_index * CEN_DEV + local_index
    subkeys = jax.random.split(jax.random.fold_in(key, 14), devices_all)
    shuffle = jax.vmap(lambda subkey: jax.random.permutation(subkey, PTS_DEV))(subkeys)
    cell_index = jnp.take_along_axis(cell_index, shuffle, axis=1)
    return cell_index.reshape(-1).astype(jnp.int32)


def levels(rng, shape, cuts, low, largest):
    def one(position, parts):
        heights = jax.random.uniform(jax.random.fold_in(jax.random.fold_in(rng, 6), position), (parts,), jnp.float32, low / len(cuts), largest / len(cuts))
        return jnp.repeat(jnp.exp(heights), shape[position] // parts).reshape((-1,) + (1,) * (len(shape) - position - 1))

    factor_of = one(*cuts[0])
    for cut in cuts[1:]:
        factor_of = factor_of * one(*cut)
    return factor_of


def centred(stream_key, dims, scale, bound, cuts=(), kind=jnp.bfloat16):
    loudness = levels(stream_key, dims, cuts, -0.22, 0.18) if cuts else 1.0
    array = jax.random.normal(stream_key, dims, jnp.float32) * scale * loudness
    return jnp.minimum(jnp.maximum(array, -bound), bound).astype(kind)


def setup_inputs(seed: int = 0) -> dict:
    key_of = jax.random.split(jax.random.key(seed), 5)
    return {
        "points": centred(key_of[0], (POINTS, D), 1.0, 6.0, ((0, 768),), jnp.float32),
        "centroids": centred(key_of[1], (CENTROIDS, D), 1.0, 6.0, ((0, 768),), jnp.float32),
        "counts": jnp.clip(jnp.exp(math.log(20.0) - 2.9957323 * jax.random.uniform(key_of[2], (CENTROIDS,), jnp.float32) ** levels(key_of[2], (CENTROIDS,), ((0, 768),), -0.2, 0.2)), 1.0, 20.0),
        "assign": draw_assign(jax.random.fold_in(key_of[4], 71), 0),
    }


def reference(points, centroids, counts, assign):
    points_low = points.astype(jnp.bfloat16)
    centroids_low = centroids.astype(jnp.bfloat16)
    cen_sq = jnp.sum(jnp.square(centroids_low.astype(jnp.float32)), axis=1)
    pts_sq = jnp.sum(points * points, axis=1)
    row_block = math.gcd(POINTS, 512)

    def nearest_block(portion):
        scores = jnp.dot(portion, centroids_low.T, preferred_element_type=jnp.float32)
        return jnp.min(cen_sq[None, :] - 2.0 * scores, axis=1)

    closest = lax.map(nearest_block, points_low.reshape(POINTS // row_block, row_block, D)).reshape(POINTS)
    nearest = (pts_sq + closest) / D
    cell_index = jnp.arange(POINTS, dtype=jnp.int32) // (N_GRP * PTS_DEV)
    target = cell_index * K_CELL + assign
    totals = jax.ops.segment_sum(points, target, num_segments=CENTROIDS)
    arrivals = jax.ops.segment_sum(jnp.ones((POINTS,), jnp.float32), target, num_segments=CENTROIDS)
    new_counts = counts + arrivals
    new_centroids = (counts[:, None] * centroids + totals) / new_counts[:, None]
    return nearest, new_centroids, new_counts
```

```python
import jax
import jax.numpy as jnp
from jax import lax
from jax.sharding import PartitionSpec as P


def on_device(points, centroids, counts, assign):
    pts_rows = points.shape[0]
    feature_width = points.shape[1]
    cen_rows = centroids.shape[0]
    blocks = lax.axis_size("blk")
    points_low = points.astype(jnp.bfloat16)
    centroids_low = centroids.astype(jnp.bfloat16)
    point_norms = jnp.sum(points * points, axis=1)
    cen_norms = jnp.sum(jnp.square(centroids_low.astype(jnp.float32)), axis=1)

    all_points = lax.all_gather(points_low, "blk", axis=0, tiled=True)
    cell_low = lax.all_gather(centroids_low, "grp", axis=0, tiled=True)
    cell_norms = lax.all_gather(cen_norms, "grp", axis=0, tiled=True)
    scores = lax.dot_general(
        all_points, cell_low, (((1,), (1,)), ((), ())), preferred_element_type=jnp.float32
    )
    partial_value = jnp.min(cell_norms[None, :] - 2.0 * scores, axis=1)
    exchanged = lax.all_to_all(
        partial_value.reshape(blocks, pts_rows), "blk", split_axis=0, concat_axis=0, tiled=True
    )
    own_rows = jnp.min(exchanged, axis=0)
    nearest = (point_norms + own_rows) / feature_width

    cell_points = lax.all_gather(points_low, "grp", axis=0, tiled=True)
    cell_assign = lax.all_gather(assign, "grp", axis=0, tiled=True)
    local_index = cell_assign - lax.axis_index("grp") * cen_rows
    matches = local_index[None, :] == jnp.arange(cen_rows, dtype=jnp.int32)[:, None]
    totals = jnp.dot(
        matches.astype(jnp.bfloat16), cell_points, preferred_element_type=jnp.float32
    )
    arrivals = jnp.sum(matches.astype(jnp.float32), axis=1)
    new_counts = counts + arrivals
    new_centroids = (counts[:, None] * centroids + totals) / new_counts[:, None]
    return (nearest, new_centroids, new_counts)


def solution(mesh):
    return jax.shard_map(
        on_device,
        mesh=mesh,
        in_specs=(
            P(("blk", "grp"), None),
            P(("blk", "grp"), None),
            P(("blk", "grp")),
            P(("blk", "grp")),
        ),
        out_specs=(P(("blk", "grp")), P(("blk", "grp"), None), P(("blk", "grp"))),
        check_vma=False,
    )
```

```python
import jax
import jax.numpy as jnp
import numpy as np
from jax import lax
from jax.sharding import Mesh
from jax.sharding import PartitionSpec as P

PT_GATHER = "split"
GRP_GATHER = "xla"
MIN_EX = "a2a"
AXES = ("y", "z", "x", "c")
ALL = AXES


def gather_grp(block):
    if GRP_GATHER == "xla":
        return lax.all_gather(block, ("x", "c"), axis=0, tiled=False)
    n = lax.axis_size(("x", "c"))
    me = lax.axis_index(("x", "c"))
    pieces = [block]
    for k in range(1, n):
        perm = [(j, (j + k) % n) for j in range(n)]
        pieces.append(lax.ppermute(block, ("x", "c"), perm))
    stacked = jnp.stack(pieces)
    order = (me - jnp.arange(n)) % n
    inv = jnp.zeros((n,), jnp.int32).at[order].set(jnp.arange(n, dtype=jnp.int32))
    return jnp.take(stacked, inv, axis=0)


def on_device(points, centroids, counts, assign):
    pts_rows, feature_width = points.shape
    cen_rows = centroids.shape[0]
    n_y = lax.axis_size("y")
    n_z = lax.axis_size("z")
    points_low = points.astype(jnp.bfloat16)
    centroids_low = centroids.astype(jnp.bfloat16)
    point_norms = jnp.sum(points * points, axis=1)

    if PT_GATHER == "split":
        all_points = lax.all_gather(lax.all_gather(points_low, "z", axis=0, tiled=True), "y", axis=0, tiled=True)
    else:
        all_points = lax.all_gather(points_low, ("y", "z"), axis=0, tiled=True)

    hi = (assign // 64).astype(jnp.bfloat16)
    lo = (assign % 64).astype(jnp.bfloat16)
    code = jnp.concatenate([hi, lo, jnp.zeros((feature_width - 2 * pts_rows,), jnp.bfloat16)])[None, :]
    block = jnp.concatenate([centroids_low, points_low, code], axis=0)
    grp_all = gather_grp(block)
    n_grp = grp_all.shape[0]
    cell_low = grp_all[:, :cen_rows].reshape(n_grp * cen_rows, feature_width)
    cell_points = grp_all[:, cen_rows:cen_rows + pts_rows].reshape(n_grp * pts_rows, feature_width)
    codes = grp_all[:, cen_rows + pts_rows].astype(jnp.int32)
    cell_assign = (codes[:, :pts_rows] * 64 + codes[:, pts_rows:2 * pts_rows]).reshape(-1)
    cell_norms = jnp.sum(jnp.square(cell_low.astype(jnp.float32)), axis=1)

    scores = lax.dot_general(all_points, cell_low, (((1,), (1,)), ((), ())), preferred_element_type=jnp.float32)
    partial_value = jnp.min(cell_norms[None, :] - 2.0 * scores, axis=1)
    if MIN_EX == "a2a2":
        pv = partial_value.reshape(n_y, n_z, pts_rows)
        s1 = lax.all_to_all(pv, "z", split_axis=1, concat_axis=1, tiled=True)
        m1 = jnp.min(s1, axis=1)
        s2 = lax.all_to_all(m1, "y", split_axis=0, concat_axis=0, tiled=True)
        own_rows = jnp.min(s2, axis=0)
    elif MIN_EX == "a2a":
        s = lax.all_to_all(partial_value.reshape(n_y * n_z, pts_rows), ("y", "z"), split_axis=0, concat_axis=0, tiled=True)
        own_rows = jnp.min(s, axis=0)
    else:
        full = lax.pmin(partial_value, ("y", "z"))
        own_rows = lax.dynamic_slice_in_dim(full, lax.axis_index(("y", "z")) * pts_rows, pts_rows)
    nearest = (point_norms + own_rows) / feature_width

    local_index = cell_assign - lax.axis_index(("x", "c")) * cen_rows
    matches = local_index[None, :] == jnp.arange(cen_rows, dtype=jnp.int32)[:, None]
    totals = jnp.dot(matches.astype(jnp.bfloat16), cell_points, preferred_element_type=jnp.float32)
    arrivals = jnp.sum(matches.astype(jnp.float32), axis=1)
    new_counts = counts + arrivals
    new_centroids = (counts[:, None] * centroids + totals) / new_counts[:, None]
    return (nearest, new_centroids, new_counts)


def solution(mesh):
    devs = np.asarray(mesh.devices)
    flat = devs.reshape(-1)
    n_y = len({d.coords[1] for d in flat})
    n_z = len({d.coords[2] for d in flat})
    n_x = len({d.coords[0] for d in flat})
    split = Mesh(devs.reshape(n_y, n_z, n_x, flat.size // (n_y * n_z * n_x)), AXES)
    row = P(ALL, None)
    vec = P(ALL)
    return jax.shard_map(on_device, mesh=split, in_specs=(row, row, vec, vec), out_specs=(vec, row, vec), check_vma=False)
```

```python
import jax
import jax.numpy as jnp
import numpy as np
from jax import lax
from jax.sharding import Mesh
from jax.sharding import PartitionSpec as P

AXES = ("y", "z", "x", "c")
STAGES = ("z", ("x", "c"))


def on_device(points, centroids, counts, assign):
    pts_rows, feature_width = points.shape
    cen_rows = centroids.shape[0]
    sizes = {a: lax.axis_size(a) for a in ("z", "x", "c")}
    points_low = points.astype(jnp.bfloat16)
    centroids_low = centroids.astype(jnp.bfloat16)
    point_norms = jnp.sum(points * points, axis=1)

    all_points = points_low
    for axis in STAGES:
        all_points = lax.all_gather(all_points, axis, axis=0, tiled=True)
    order = tuple(a for axis in reversed(STAGES) for a in ((axis,) if isinstance(axis, str) else axis))
    slice_low = lax.all_gather(centroids_low, "y", axis=0, tiled=True)
    slice_norms = jnp.sum(jnp.square(slice_low.astype(jnp.float32)), axis=1)

    scores = lax.dot_general(all_points, slice_low, (((1,), (1,)), ((), ())), preferred_element_type=jnp.float32)
    partial_value = jnp.min(slice_norms[None, :] - 2.0 * scores, axis=1)
    shaped = partial_value.reshape(tuple(sizes[a] for a in order) + (pts_rows,))
    perm = tuple(order.index(a) for a in ("z", "x", "c")) + (len(order),)
    rows = shaped.transpose(perm).reshape(-1, pts_rows)
    exchanged = lax.all_to_all(rows, ("z", "x", "c"), split_axis=0, concat_axis=0, tiled=True)
    own_rows = jnp.min(exchanged, axis=0)
    nearest = (point_norms + own_rows) / feature_width

    mine = shaped.shape[:-1]
    cell = all_points.reshape(mine + (pts_rows, feature_width))
    cell = jnp.take(cell, lax.axis_index("z"), axis=order.index("z"))
    rest = tuple(a for a in order if a != "z")
    cell = cell.transpose(tuple(rest.index(a) for a in ("x", "c")) + (2, 3)).reshape(-1, feature_width)
    cell_assign = lax.all_gather(assign, ("x", "c"), axis=0, tiled=True)
    local_index = cell_assign - lax.axis_index(("x", "c")) * cen_rows
    matches = local_index[None, :] == jnp.arange(cen_rows, dtype=jnp.int32)[:, None]
    totals = jnp.dot(matches.astype(jnp.bfloat16), cell, preferred_element_type=jnp.float32)
    arrivals = jnp.sum(matches.astype(jnp.float32), axis=1)
    new_counts = counts + arrivals
    new_centroids = (counts[:, None] * centroids + totals) / new_counts[:, None]
    return (nearest, new_centroids, new_counts)


def solution(mesh):
    devs = np.asarray(mesh.devices)
    flat = devs.reshape(-1)
    n_y = len({d.coords[1] for d in flat})
    n_z = len({d.coords[2] for d in flat})
    n_x = len({d.coords[0] for d in flat})
    split = Mesh(devs.reshape(n_y, n_z, n_x, flat.size // (n_y * n_z * n_x)), AXES)
    row = P(AXES, None)
    vec = P(AXES)
    return jax.shard_map(on_device, mesh=split, in_specs=(row, row, vec, vec), out_specs=(vec, row, vec), check_vma=False)
```

```python
import jax
import jax.numpy as jnp
import numpy as np
from jax import lax
from jax.sharding import Mesh
from jax.sharding import PartitionSpec as P

AXES = ("y", "z", "x", "c")
STAGES = ("z", ("x", "c"))


def gather_by_a2a(block, axis):
    n = lax.axis_size(axis)
    spread = jnp.broadcast_to(block[None], (n,) + block.shape)
    got = lax.all_to_all(spread, axis, split_axis=0, concat_axis=0, tiled=True)
    return got.reshape((n * block.shape[0],) + block.shape[1:])


def on_device(points, centroids, counts, assign):
    pts_rows, feature_width = points.shape
    cen_rows = centroids.shape[0]
    sizes = {a: lax.axis_size(a) for a in ("z", "x", "c")}
    points_low = points.astype(jnp.bfloat16)
    centroids_low = centroids.astype(jnp.bfloat16)
    point_norms = jnp.sum(points * points, axis=1)

    all_points = points_low
    for axis in STAGES:
        if axis == "z":
            all_points = gather_by_a2a(all_points, axis)
        else:
            all_points = lax.all_gather(all_points, axis, axis=0, tiled=True)
    order = tuple(a for axis in reversed(STAGES) for a in ((axis,) if isinstance(axis, str) else axis))
    slice_low = gather_by_a2a(centroids_low, "y")
    slice_norms = jnp.sum(jnp.square(slice_low.astype(jnp.float32)), axis=1)

    scores = lax.dot_general(all_points, slice_low, (((1,), (1,)), ((), ())), preferred_element_type=jnp.float32)
    partial_value = jnp.min(slice_norms[None, :] - 2.0 * scores, axis=1)
    shaped = partial_value.reshape(tuple(sizes[a] for a in order) + (pts_rows,))
    perm = tuple(order.index(a) for a in ("z", "x", "c")) + (len(order),)
    rows = shaped.transpose(perm).reshape(-1, pts_rows)
    exchanged = lax.all_to_all(rows, ("z", "x", "c"), split_axis=0, concat_axis=0, tiled=True)
    own_rows = jnp.min(exchanged, axis=0)
    nearest = (point_norms + own_rows) / feature_width

    mine = shaped.shape[:-1]
    cell = all_points.reshape(mine + (pts_rows, feature_width))
    cell = jnp.take(cell, lax.axis_index("z"), axis=order.index("z"))
    rest = tuple(a for a in order if a != "z")
    cell = cell.transpose(tuple(rest.index(a) for a in ("x", "c")) + (2, 3)).reshape(-1, feature_width)
    cell_assign = lax.all_gather(assign, ("x", "c"), axis=0, tiled=True)
    local_index = cell_assign - lax.axis_index(("x", "c")) * cen_rows
    matches = local_index[None, :] == jnp.arange(cen_rows, dtype=jnp.int32)[:, None]
    totals = jnp.dot(matches.astype(jnp.bfloat16), cell, preferred_element_type=jnp.float32)
    arrivals = jnp.sum(matches.astype(jnp.float32), axis=1)
    new_counts = counts + arrivals
    new_centroids = (counts[:, None] * centroids + totals) / new_counts[:, None]
    return (nearest, new_centroids, new_counts)


def solution(mesh):
    devs = np.asarray(mesh.devices)
    flat = devs.reshape(-1)
    n_y = len({d.coords[1] for d in flat})
    n_z = len({d.coords[2] for d in flat})
    n_x = len({d.coords[0] for d in flat})
    split = Mesh(devs.reshape(n_y, n_z, n_x, flat.size // (n_y * n_z * n_x)), AXES)
    row = P(AXES, None)
    vec = P(AXES)
    return jax.shard_map(on_device, mesh=split, in_specs=(row, row, vec, vec), out_specs=(vec, row, vec), check_vma=False)
```
